768 devices in a mesh: section: 4 (over y_hi, core), dp: 48 (over x, z), sp: 4 (over y_lo).
Axes of the slice: x: 4, y: 8 (y_hi: 2, y_lo: 4; y = y_hi * 4 + y_lo), z: 12, core: 2. Of those that a mesh axis runs over, the one named last changes fastest.
Arguments:
- projected: bfloat16 [4, 48, 512, 3, 24, 128], P('section', 'dp', 'sp'), may hold values from -100 to 100, as said below
- seg_ids: int32 [4, 48, 512], P('section', 'dp'), may hold values from 0 to 7, never falling along the last dimension, each value on 1 to 128 neighbouring positions
- condition: bfloat16 [4, 384, 3072], P('section', 'dp'), may hold values from -8 to 8
- w_gate: bfloat16 [4, 3072, 3072], P('section', 'dp'), may hold values from -0.109375 to 0.109375
Outputs:
- handed: bfloat16 [4, 48, 512, 3072], P('section', 'dp', 'sp')
The draws below stay inside these ranges and needn't reach their ends.
Inputs may be any that keep to these rules, and one draw needn't show every extreme that they name: `projected`: Query, key and value entries lie within the range. `seg_ids`: within a row the sample numbers never fall; each of the 8 samples holds 1 to 128 positions and one holds exactly 128.
All inputs are finite; a program needn't handle non-finite values.
Results may differ from the reference program's by a relative error of at most 0.006.
Values may be sent and summed in bfloat16 or wider, within the bound.
No kernel may reach another device: no remote copies, remote signals or barrier semaphores. Data moves between devices by JAX's collectives and lax.ppermute only.
A program may use at most 32 MiB of HBM per device.

```python
import math
import jax
import jax.numpy as jnp
import numpy as np
from jax import lax

H = 24
HD = 128
D = 3072
L = 512
SEG = 8
SEGLEN = 128
N_SECTION = 4
N_DP = 48


def draw_projected(key, part):
    first_key = jax.random.fold_in(key, 0)
    shape = (N_SECTION, N_DP, L, 3, H, HD)
    base = jnp.clip(jax.random.normal(first_key, shape, jnp.float32), -4.0, 4.0)
    factor = jnp.array([1.3, 1.3, 1.0], jnp.float32).reshape(1, 1, 1, 3, 1, 1)
    base = base * factor
    query_rows = base[:, :, :, 0]
    key_rows = base[:, :, :, 1]
    values = base[:, :, :, 2]
    stacked = jnp.stack([query_rows, key_rows, values], axis=3)
    return stacked.astype(jnp.bfloat16)


def levels(key, shape, cuts, low, high):
    def one(dim, shards_of):
        steps = jax.random.uniform(jax.random.fold_in(jax.random.fold_in(key, 6), dim), (shards_of,), jnp.float32, low / len(cuts), high / len(cuts))
        return jnp.repeat(jnp.exp(steps), shape[dim] // shards_of).reshape((-1,) + (1,) * (len(shape) - dim - 1))

    gain = one(*cuts[0])
    for cut in cuts[1:]:
        gain = gain * one(*cut)
    return gain


def profile(amount, total, bound, skew):
    loads = [(1 << 20) // math.isqrt(grade ** skew) + 1 for grade in range(2, amount + 1)]
    surplus, counts = total - bound - (amount - 1), [1] * (amount - 1)
    while surplus > 0:
        candidates = [i for i in range(amount - 1) if counts[i] < bound]
        mass, left = sum([loads[i] for i in candidates]), surplus
        for i in candidates:
            addition = min(bound - counts[i], max(1, left * loads[i] // mass), surplus)
            counts[i] = counts[i] + addition
            surplus = surplus - addition
    return np.array([bound] + counts)


def uneven_parts(key, count, total, reach, skew):
    if count == 2:
        one = jax.random.randint(key, (), max(1, total - reach), min(reach, total - 1) + 1)
        return jnp.stack([one, total - one])
    sizes = jnp.asarray(profile(count, total, reach, skew), jnp.int32)
    pairs = (count - 1) // 2
    donor, sink = sizes[1:1 + 2 * pairs:2], sizes[2:2 + 2 * pairs:2]
    slack = jnp.minimum(donor - 1, reach - sink)
    moved = jax.random.randint(jax.random.fold_in(key, 1), (pairs,), 0, 1 << 20) % (slack + 1)
    sizes = sizes.at[1:1 + 2 * pairs:2].set(donor - moved).at[2:2 + 2 * pairs:2].set(sink + moved)
    return sizes[jax.random.permutation(jax.random.fold_in(key, 2), count)]


def bell_draw(stream_key, extent, spread, limit, cuts=(), kind=jnp.bfloat16):
    result = spread * jax.random.normal(stream_key, extent, jnp.float32)
    if cuts:
        result = result * levels(stream_key, extent, cuts, -0.22, 0.18)
    return jnp.clip(result, -limit, limit).astype(kind)


def setup_inputs(seed: int = 0) -> dict:
    seeds = jax.random.split(jax.random.key(seed), 5)
    projected = draw_projected(jax.random.fold_in(seeds[4], 71), 0)
    seg_ids = jax.vmap(lambda own: jnp.searchsorted(jnp.cumsum(uneven_parts(own, SEG, L, SEGLEN, 2)), jnp.arange(L), side="right"))(jax.random.split(seeds[1], N_SECTION * N_DP)).reshape((N_SECTION, N_DP, L)).astype(jnp.int32)
    condition = bell_draw(seeds[2], (N_SECTION, N_DP * SEG, D), 2.0, 8.0, ((0, 4), (1, 48)))
    w_gate = bell_draw(seeds[3], (N_SECTION, D, D), D ** -0.5, 0.109375, ((0, 4), (1, 48)))
    return dict(projected=projected, seg_ids=seg_ids, condition=condition, w_gate=w_gate)


masked_score = -1e+30

def attend_row(exchanged, segment_row):
    query_rows = exchanged[:, 0]
    key_rows = exchanged[:, 1].astype(jnp.float32)
    values = exchanged[:, 2].astype(jnp.float32)
    length = query_rows.shape[0]
    query_block = min(512, length)
    block_count = length // query_block
    scale_factor = 1.0 / math.sqrt(query_rows.shape[2])

    def one_block(block_index):
        first_row = block_index * query_block
        query_part = lax.dynamic_slice_in_dim(query_rows, first_row, query_block, 0).astype(jnp.float32)
        seg_part = lax.dynamic_slice_in_dim(segment_row, first_row, query_block, 0)
        scores = jnp.einsum('qhd,khd->hqk', query_part, key_rows) * scale_factor
        same_segment = seg_part[:, None] == segment_row[None, :]
        scores = jnp.where(same_segment[None], scores, masked_score)
        row_max = lax.optimization_barrier(jnp.max(scores, axis=2, keepdims=True))
        weights = jnp.exp(scores - row_max)
        row_total = lax.optimization_barrier(jnp.sum(weights, axis=2, keepdims=True))
        rounded = weights.astype(jnp.bfloat16)
        mixed_out = jnp.einsum('hqk,khd->qhd', rounded.astype(jnp.float32), values)
        mixed_out = mixed_out / jnp.transpose(row_total, (1, 0, 2))
        return mixed_out.astype(jnp.bfloat16)
    blocks = lax.map(one_block, jnp.arange(block_count, dtype=jnp.int32))
    return blocks.reshape(length, blocks.shape[2], blocks.shape[3])

def reference(projected, seg_ids, condition, w_gate):
    section_outputs = []
    for section_number in range(N_SECTION):
        cond_act = jax.nn.silu(condition[section_number].astype(jnp.float32)).astype(jnp.bfloat16)
        seg_gate = jnp.dot(cond_act, w_gate[section_number], preferred_element_type=jnp.float32)
        seg_gate = seg_gate.reshape(N_DP, SEG, H * HD)

        def one_row(inputs):
            rows, segment_row, gates = inputs
            attended = attend_row(rows, segment_row).reshape(L, H * HD)
            one_hot = (segment_row[:, None] == jnp.arange(SEG, dtype=jnp.int32)[None, :]).astype(jnp.float32)
            token_gate = jnp.dot(one_hot, gates, precision=lax.Precision.HIGHEST)
            return (token_gate * attended.astype(jnp.float32)).astype(jnp.bfloat16)
        section_outputs.append(lax.map(one_row, (projected[section_number], seg_ids[section_number], seg_gate)))
    gated = jnp.stack(section_outputs)
    return jnp.roll(gated, 1, axis=0)
```

```python
import math

import jax
import jax.numpy as jnp
from jax import lax
from jax.sharding import Mesh, PartitionSpec as P

masked_score = -1e30


def from_behind(block, axis, distance):
    devices = range(lax.axis_size(axis))
    route = [((i - distance) % len(devices), i) for i in devices]
    return lax.ppermute(block, axis, route)


def attend_row(exchanged, segment_row):
    query_rows = exchanged[:, 0]
    key_rows = exchanged[:, 1]
    values = exchanged[:, 2]
    length = query_rows.shape[0]
    query_block = min(512, length)
    block_count = length // query_block
    scale_factor = 1.0 / math.sqrt(query_rows.shape[2])

    def one_block(block_index):
        scores = (
            jnp.einsum("qhd,khd->hqk", query_rows, key_rows, preferred_element_type=jnp.float32)
            * scale_factor
        )
        same_segment = segment_row[:, None] == segment_row[None, :]
        scores = jnp.where(same_segment[None], scores, masked_score)
        row_max = jnp.max(scores, axis=2, keepdims=True)
        weights = jnp.exp(scores - row_max)
        row_total = jnp.sum(weights, axis=2, keepdims=True)
        rounded = weights.astype(jnp.bfloat16)
        mixed_out = jnp.einsum("hqk,khd->qhd", rounded, values, preferred_element_type=jnp.float32)
        mixed_out = mixed_out / jnp.transpose(row_total, (1, 0, 2))
        return mixed_out.astype(jnp.bfloat16)

    blocks = lax.map(one_block, jnp.arange(block_count, dtype=jnp.int32))
    return blocks.reshape(length, blocks.shape[2], blocks.shape[3])


def sample_gates(cond, rows_weight):
    seg_count, model_width = cond.shape
    row_count = rows_weight.shape[0]
    nx = lax.axis_size("dx")
    nz = lax.axis_size("dz")
    col_block = model_width // nz
    cond_act = jax.nn.silu(cond.astype(jnp.float32)).astype(jnp.bfloat16)
    w_cols = lax.all_to_all(
        rows_weight.reshape(row_count, nz, col_block), "dz", split_axis=1, concat_axis=0, tiled=True
    ).reshape(nz * row_count, col_block)
    feat = lax.all_to_all(
        cond_act.reshape(seg_count, nx, model_width // nx), "dx", split_axis=1, concat_axis=0, tiled=True
    ).reshape(nx * seg_count, model_width // nx)
    feat = lax.all_gather(feat, "dz", axis=0, tiled=True)
    partial = jnp.dot(feat, w_cols, preferred_element_type=jnp.float32)
    partial = partial.reshape(nz, nx, seg_count, col_block)
    summed = lax.psum_scatter(partial, "dx", scatter_dimension=1, tiled=True)
    gathered = lax.all_to_all(summed, "dz", split_axis=0, concat_axis=1, tiled=True)
    return jnp.transpose(gathered.reshape(nz, seg_count, col_block), (1, 0, 2)).reshape(
        seg_count, model_width
    )


def shards(projected, seg_ids, condition, w_gate):
    tok_rows = projected.shape[2]
    head_count = projected.shape[4]
    head_size = projected.shape[5]
    model_width = head_count * head_size
    group_count = lax.axis_size("sp")
    joined_rows = projected.reshape(tok_rows, 3, group_count, head_count // group_count, head_size)
    segment_row = seg_ids.reshape(-1)
    attended = attend_row(
        lax.all_to_all(joined_rows, "sp", split_axis=2, concat_axis=0, tiled=True)[:, :, 0],
        segment_row,
    )
    merged = lax.all_to_all(attended, "sp", split_axis=0, concat_axis=1, tiled=True).reshape(
        tok_rows, model_width
    )
    seg_gate = sample_gates(condition[0], w_gate[0])
    local_segments = lax.dynamic_slice_in_dim(
        segment_row, lax.axis_index("sp") * tok_rows, tok_rows, 0
    )
    seg_count = seg_gate.shape[0]
    one_hot = (local_segments[:, None] == jnp.arange(seg_count, dtype=jnp.int32)[None, :]).astype(
        jnp.float32
    )
    token_gate = jnp.dot(one_hot, seg_gate, precision=lax.Precision.HIGHEST)
    gated_out = (token_gate * merged.astype(jnp.float32)).astype(jnp.bfloat16)
    handed = from_behind(gated_out, "section", 1)
    return handed.reshape(1, 1, tok_rows, model_width)


def solution(mesh):
    n_section, n_dp, n_sp = (mesh.shape[a] for a in ("section", "dp", "sp"))
    n_x = 4 if n_dp % 4 == 0 else 1
    split_mesh = Mesh(
        mesh.devices.reshape(n_section, n_x, n_dp // n_x, n_sp), ("section", "dx", "dz", "sp")
    )
    dp = ("dx", "dz")
    placed = (
        P("section", dp, "sp", None, None, None),
        P("section", dp, None),
        P("section", dp, None),
        P("section", dp, None),
    )
    return jax.shard_map(
        shards,
        mesh=split_mesh,
        in_specs=placed,
        out_specs=P("section", dp, "sp", None),
        check_vma=False,
    )
```

```python
import math

import jax
import jax.numpy as jnp
from jax import lax
from jax.sharding import Mesh, PartitionSpec as P

masked_score = -1e30


def from_behind(block, axis, distance):
    devices = range(lax.axis_size(axis))
    route = [((i - distance) % len(devices), i) for i in devices]
    return lax.ppermute(block, axis, route)


def neighbour_keys(kv, axis):
    count = lax.axis_size(axis)
    from_left = lax.ppermute(kv, axis, [(i, i + 1) for i in range(count - 1)])
    from_right = lax.ppermute(kv, axis, [(i + 1, i) for i in range(count - 1)])
    return jnp.concatenate([from_left, kv, from_right], axis=0)


def attend_chunk(local, segment_row, axis):
    rows = local.shape[0]
    chunk = lax.axis_index(axis)
    total_rows = segment_row.shape[0]
    query_rows = local[:, 0]
    keys = neighbour_keys(local[:, 1:3], axis)
    key_rows = keys[:, 0]
    values = keys[:, 1]
    scale_factor = 1.0 / math.sqrt(query_rows.shape[2])
    query_seg = lax.dynamic_slice_in_dim(segment_row, chunk * rows, rows, 0)
    key_pos = (chunk - 1) * rows + jnp.arange(3 * rows, dtype=jnp.int32)
    key_valid = (key_pos >= 0) & (key_pos < total_rows)
    key_seg = jnp.take(segment_row, jnp.clip(key_pos, 0, total_rows - 1), axis=0)
    same_segment = (query_seg[:, None] == key_seg[None, :]) & key_valid[None, :]
    scores = (
        jnp.einsum("qhd,khd->hqk", query_rows, key_rows, preferred_element_type=jnp.float32)
        * scale_factor
    )
    scores = jnp.where(same_segment[None], scores, masked_score)
    row_max = jnp.max(scores, axis=2, keepdims=True)
    weights = jnp.exp(scores - row_max)
    row_total = jnp.sum(weights, axis=2, keepdims=True)
    rounded = weights.astype(jnp.bfloat16)
    mixed_out = jnp.einsum("hqk,khd->qhd", rounded, values, preferred_element_type=jnp.float32)
    mixed_out = mixed_out / jnp.transpose(row_total, (1, 0, 2))
    return mixed_out.astype(jnp.bfloat16), query_seg


def sample_gates(cond, rows_weight):
    dp = ("dx", "dz")
    seg_count, model_width = cond.shape
    row_count = rows_weight.shape[0]
    nx = lax.axis_size("dx")
    nz = lax.axis_size("dz")
    col_block = model_width // nz
    feat_block = model_width // nx
    cond_act = jax.nn.silu(cond.astype(jnp.float32)).astype(jnp.bfloat16)
    w_cols = lax.all_to_all(
        rows_weight.reshape(row_count, nz, col_block), "dz", split_axis=1, concat_axis=0, tiled=True
    ).reshape(nz * row_count, col_block)
    sent = jnp.transpose(cond_act.reshape(seg_count, nx, feat_block), (1, 0, 2))
    sent = jnp.broadcast_to(sent[:, None], (nx, nz, seg_count, feat_block))
    feat = lax.all_to_all(
        sent.reshape(nx * nz, seg_count, feat_block), dp, split_axis=0, concat_axis=0, tiled=True
    ).reshape(nx * nz * seg_count, feat_block)
    partial = jnp.dot(feat, w_cols, preferred_element_type=jnp.float32)
    parts = lax.all_to_all(
        partial.reshape(nx * nz, seg_count, col_block), dp, split_axis=0, concat_axis=0, tiled=True
    ).reshape(nx, nz, seg_count, col_block)
    summed = jnp.sum(parts, axis=0)
    return jnp.transpose(summed, (1, 0, 2)).reshape(seg_count, model_width)


def shards(projected, seg_ids, condition, w_gate):
    tok_rows = projected.shape[2]
    head_count = projected.shape[4]
    head_size = projected.shape[5]
    model_width = head_count * head_size
    segment_row = seg_ids.reshape(-1)
    attended, local_segments = attend_chunk(projected[0, 0], segment_row, "sp")
    merged = attended.reshape(tok_rows, model_width)
    seg_gate = sample_gates(condition[0], w_gate[0])
    seg_count = seg_gate.shape[0]
    one_hot = (local_segments[:, None] == jnp.arange(seg_count, dtype=jnp.int32)[None, :]).astype(
        jnp.float32
    )
    token_gate = jnp.dot(one_hot, seg_gate, precision=lax.Precision.HIGHEST)
    gated_out = (token_gate * merged.astype(jnp.float32)).astype(jnp.bfloat16)
    handed = from_behind(gated_out, "section", 1)
    return handed.reshape(1, 1, tok_rows, model_width)


def solution(mesh):
    n_section, n_dp, n_sp = (mesh.shape[a] for a in ("section", "dp", "sp"))
    n_x = 4 if n_dp % 4 == 0 else 1
    split_mesh = Mesh(
        mesh.devices.reshape(n_section, n_x, n_dp // n_x, n_sp), ("section", "dx", "dz", "sp")
    )
    dp = ("dx", "dz")
    placed = (
        P("section", dp, "sp", None, None, None),
        P("section", dp, None),
        P("section", dp, None),
        P("section", dp, None),
    )
    return jax.shard_map(
        shards,
        mesh=split_mesh,
        in_specs=placed,
        out_specs=P("section", dp, "sp", None),
        check_vma=False,
    )
```

```python
import math

import jax
import jax.numpy as jnp
from jax import lax
from jax.sharding import Mesh, PartitionSpec as P

masked_score = -1e30


def from_behind(block, axis, distance):
    devices = range(lax.axis_size(axis))
    route = [((i - distance) % len(devices), i) for i in devices]
    return lax.ppermute(block, axis, route)


def neighbour_keys(kv, axis):
    count = lax.axis_size(axis)
    from_left = lax.ppermute(kv, axis, [(i, i + 1) for i in range(count - 1)])
    from_right = lax.ppermute(kv, axis, [(i + 1, i) for i in range(count - 1)])
    return jnp.concatenate([from_left, kv, from_right], axis=0)


def attend_chunk(local, segment_row, axis):
    rows = local.shape[0]
    chunk = lax.axis_index(axis)
    total_rows = segment_row.shape[0]
    query_rows = local[:, 0]
    keys = neighbour_keys(local[:, 1:3], axis)
    key_rows = keys[:, 0]
    values = keys[:, 1]
    scale_factor = 1.0 / math.sqrt(query_rows.shape[2])
    query_seg = lax.dynamic_slice_in_dim(segment_row, chunk * rows, rows, 0)
    key_pos = (chunk - 1) * rows + jnp.arange(3 * rows, dtype=jnp.int32)
    key_valid = (key_pos >= 0) & (key_pos < total_rows)
    key_seg = jnp.take(segment_row, jnp.clip(key_pos, 0, total_rows - 1), axis=0)
    same_segment = (query_seg[:, None] == key_seg[None, :]) & key_valid[None, :]
    scores = (
        jnp.einsum("qhd,khd->hqk", query_rows, key_rows, preferred_element_type=jnp.float32)
        * scale_factor
    )
    scores = jnp.where(same_segment[None], scores, masked_score)
    row_max = jnp.max(scores, axis=2, keepdims=True)
    weights = jnp.exp(scores - row_max)
    row_total = jnp.sum(weights, axis=2, keepdims=True)
    rounded = weights.astype(jnp.bfloat16)
    mixed_out = jnp.einsum("hqk,khd->qhd", rounded, values, preferred_element_type=jnp.float32)
    mixed_out = mixed_out / jnp.transpose(row_total, (1, 0, 2))
    return mixed_out.astype(jnp.bfloat16), query_seg


def sample_gates(cond, rows_weight):
    dp = ("dx", "dz")
    seg_count, model_width = cond.shape
    row_count = rows_weight.shape[0]
    nx = lax.axis_size("dx")
    nz = lax.axis_size("dz")
    col_block = model_width // nz
    feat_block = model_width // nx
    cond_act = jax.nn.silu(cond.astype(jnp.float32)).astype(jnp.bfloat16)
    w_cols = lax.all_to_all(
        rows_weight.reshape(row_count, nz, col_block), "dz", split_axis=1, concat_axis=0, tiled=True
    ).reshape(nz * row_count, col_block)
    sent = jnp.transpose(cond_act.reshape(seg_count, nx, feat_block), (1, 0, 2))
    sent = jnp.broadcast_to(sent[:, None], (nx, nz, seg_count, feat_block))
    feat = lax.all_to_all(
        sent.reshape(nx * nz, seg_count, feat_block), dp, split_axis=0, concat_axis=0, tiled=True
    ).reshape(nx * nz * seg_count, feat_block)
    partial = jnp.dot(feat, w_cols, preferred_element_type=jnp.float32)
    parts = lax.all_to_all(
        partial.reshape(nx * nz, seg_count, col_block), dp, split_axis=0, concat_axis=0, tiled=True
    ).reshape(nx, nz, seg_count, col_block)
    summed = jnp.sum(parts, axis=0)
    return jnp.transpose(summed, (1, 0, 2)).reshape(seg_count, model_width)


def shards(projected, seg_ids, condition, w_gate):
    tok_rows = projected.shape[2]
    head_count = projected.shape[4]
    head_size = projected.shape[5]
    model_width = head_count * head_size
    segment_row = seg_ids.reshape(-1)
    attended, local_segments = attend_chunk(projected[0, 0], segment_row, "sp")
    merged = attended.reshape(tok_rows, model_width)
    merged = from_behind(merged, "section", 1)
    local_segments = from_behind(local_segments, "section", 1)
    seg_gate = from_behind(sample_gates(condition[0], w_gate[0]), "section", 1)
    seg_count = seg_gate.shape[0]
    one_hot = (local_segments[:, None] == jnp.arange(seg_count, dtype=jnp.int32)[None, :]).astype(
        jnp.float32
    )
    token_gate = jnp.dot(one_hot, seg_gate, precision=lax.Precision.HIGHEST)
    handed = (token_gate * merged.astype(jnp.float32)).astype(jnp.bfloat16)
    return handed.reshape(1, 1, tok_rows, model_width)


def solution(mesh):
    n_section, n_dp, n_sp = (mesh.shape[a] for a in ("section", "dp", "sp"))
    n_x = 4 if n_dp % 4 == 0 else 1
    split_mesh = Mesh(
        mesh.devices.reshape(n_section, n_x, n_dp // n_x, n_sp), ("section", "dx", "dz", "sp")
    )
    dp = ("dx", "dz")
    placed = (
        P("section", dp, "sp", None, None, None),
        P("section", dp, None),
        P("section", dp, None),
        P("section", dp, None),
    )
    return jax.shard_map(
        shards,
        mesh=split_mesh,
        in_specs=placed,
        out_specs=P("section", dp, "sp", None),
        check_vma=False,
    )
```

```python
import math

import jax
import jax.numpy as jnp
from jax import lax
from jax.sharding import Mesh, PartitionSpec as P

masked_score = -1e30


def from_behind(block, axis, distance):
    devices = range(lax.axis_size(axis))
    route = [((i - distance) % len(devices), i) for i in devices]
    return lax.ppermute(block, axis, route)


def neighbour_keys(kv, axis):
    count = lax.axis_size(axis)
    from_left = lax.ppermute(kv, axis, [(i, i + 1) for i in range(count - 1)])
    from_right = lax.ppermute(kv, axis, [(i + 1, i) for i in range(count - 1)])
    return jnp.concatenate([from_left, kv, from_right], axis=0)


def attend_chunk(local, segment_row, axis):
    rows = local.shape[0]
    chunk = lax.axis_index(axis)
    total_rows = segment_row.shape[0]
    query_rows = local[:, 0]
    keys = neighbour_keys(local[:, 1:3], axis)
    key_rows = keys[:, 0]
    values = keys[:, 1]
    scale_factor = 1.0 / math.sqrt(query_rows.shape[2])
    query_seg = lax.dynamic_slice_in_dim(segment_row, chunk * rows, rows, 0)
    key_pos = (chunk - 1) * rows + jnp.arange(3 * rows, dtype=jnp.int32)
    key_valid = (key_pos >= 0) & (key_pos < total_rows)
    key_seg = jnp.take(segment_row, jnp.clip(key_pos, 0, total_rows - 1), axis=0)
    same_segment = (query_seg[:, None] == key_seg[None, :]) & key_valid[None, :]
    scores = (
        jnp.einsum("qhd,khd->hqk", query_rows, key_rows, preferred_element_type=jnp.float32)
        * scale_factor
    )
    scores = jnp.where(same_segment[None], scores, masked_score)
    row_max = jnp.max(scores, axis=2, keepdims=True)
    weights = jnp.exp(scores - row_max)
    row_total = jnp.sum(weights, axis=2, keepdims=True)
    rounded = weights.astype(jnp.bfloat16)
    mixed_out = jnp.einsum("hqk,khd->qhd", rounded, values, preferred_element_type=jnp.float32)
    mixed_out = mixed_out / jnp.transpose(row_total, (1, 0, 2))
    return mixed_out.astype(jnp.bfloat16), query_seg


def sample_gates(cond, rows_weight):
    dp = ("dx", "dz")
    seg_count, model_width = cond.shape
    row_count = rows_weight.shape[0]
    nx = lax.axis_size("dx")
    nz = lax.axis_size("dz")
    col_block = model_width // nz
    feat_block = model_width // nx
    cond_act = jax.nn.silu(cond.astype(jnp.float32)).astype(jnp.bfloat16)
    sent = jnp.transpose(cond_act.reshape(seg_count, nx, feat_block), (1, 0, 2))
    sent = jnp.broadcast_to(sent[:, None], (nx, nz, seg_count, feat_block))
    feat = lax.all_to_all(
        sent.reshape(nx * nz, seg_count, feat_block), dp, split_axis=0, concat_axis=0, tiled=True
    ).reshape(nx * nz * seg_count, nz, row_count)
    me = lax.axis_index("dz")
    pieces = []
    for t in range(nz):
        piece = lax.dynamic_slice_in_dim(rows_weight, ((me + t) % nz) * col_block, col_block, 1)
        if t:
            piece = lax.ppermute(piece, "dz", [(j, (j + t) % nz) for j in range(nz)])
        pieces.append(piece)
    w_cols = jnp.concatenate(pieces, axis=0)
    order = (me - jnp.arange(nz, dtype=jnp.int32)) % nz
    feat = jnp.take(feat, order, axis=1).reshape(nx * nz * seg_count, nz * row_count)
    partial = jnp.dot(feat, w_cols, preferred_element_type=jnp.float32)
    parts = lax.all_to_all(
        partial.reshape(nx * nz, seg_count, col_block), dp, split_axis=0, concat_axis=0, tiled=True
    ).reshape(nx, nz, seg_count, col_block)
    summed = jnp.sum(parts, axis=0)
    return jnp.transpose(summed, (1, 0, 2)).reshape(seg_count, model_width)


def shards(projected, seg_ids, condition, w_gate):
    tok_rows = projected.shape[2]
    head_count = projected.shape[4]
    head_size = projected.shape[5]
    model_width = head_count * head_size
    segment_row = seg_ids.reshape(-1)
    attended, local_segments = attend_chunk(projected[0, 0], segment_row, "sp")
    merged = attended.reshape(tok_rows, model_width)
    merged = from_behind(merged, "section", 1)
    local_segments = from_behind(local_segments, "section", 1)
    seg_gate = from_behind(sample_gates(condition[0], w_gate[0]), "section", 1)
    seg_count = seg_gate.shape[0]
    one_hot = (local_segments[:, None] == jnp.arange(seg_count, dtype=jnp.int32)[None, :]).astype(
        jnp.float32
    )
    token_gate = jnp.dot(one_hot, seg_gate, precision=lax.Precision.HIGHEST)
    handed = (token_gate * merged.astype(jnp.float32)).astype(jnp.bfloat16)
    return handed.reshape(1, 1, tok_rows, model_width)


def solution(mesh):
    n_section, n_dp, n_sp = (mesh.shape[a] for a in ("section", "dp", "sp"))
    n_x = 4 if n_dp % 4 == 0 else 1
    split_mesh = Mesh(
        mesh.devices.reshape(n_section, n_x, n_dp // n_x, n_sp), ("section", "dx", "dz", "sp")
    )
    dp = ("dx", "dz")
    placed = (
        P("section", dp, "sp", None, None, None),
        P("section", dp, None),
        P("section", dp, None),
        P("section", dp, None),
    )
    return jax.shard_map(
        shards,
        mesh=split_mesh,
        in_specs=placed,
        out_specs=P("section", dp, "sp", None),
        check_vma=False,
    )
```

```python
import math

import jax
import jax.numpy as jnp
from jax import lax
from jax.sharding import Mesh, PartitionSpec as P


masked_score = -1e30


def from_behind(block, axis, distance):
    devices = range(lax.axis_size(axis))
    route = [((i - distance) % len(devices), i) for i in devices]
    return lax.ppermute(block, axis, route)


def neighbour_keys(kv, axis):
    count = lax.axis_size(axis)
    from_left = lax.ppermute(kv, axis, [(i, i + 1) for i in range(count - 1)])
    from_right = lax.ppermute(kv, axis, [(i + 1, i) for i in range(count - 1)])
    return jnp.concatenate([from_left, kv, from_right], axis=0)


def attend_chunk(local, segment_row, axis):
    rows = local.shape[0]
    chunk = lax.axis_index(axis)
    total_rows = segment_row.shape[0]
    keys = neighbour_keys(local[:, 1:3], axis)
    return attend_keys(local[:, 0], keys, segment_row, chunk, rows, total_rows)


def attend_keys(query_rows, keys, segment_row, chunk, rows, total_rows):
    key_rows = keys[:, 0]
    values = keys[:, 1]
    scale_factor = 1.0 / math.sqrt(query_rows.shape[2])
    query_seg = lax.dynamic_slice_in_dim(segment_row, chunk * rows, rows, 0)
    key_pos = (chunk - 1) * rows + jnp.arange(3 * rows, dtype=jnp.int32)
    key_valid = (key_pos >= 0) & (key_pos < total_rows)
    key_seg = jnp.take(segment_row, jnp.clip(key_pos, 0, total_rows - 1), axis=0)
    same_segment = (query_seg[:, None] == key_seg[None, :]) & key_valid[None, :]
    scores = (
        jnp.einsum("qhd,khd->hqk", query_rows, key_rows, preferred_element_type=jnp.float32)
        * scale_factor
    )
    scores = jnp.where(same_segment[None], scores, masked_score)
    row_max = jnp.max(scores, axis=2, keepdims=True)
    weights = jnp.exp(scores - row_max)
    row_total = jnp.sum(weights, axis=2, keepdims=True)
    rounded = weights.astype(jnp.bfloat16)
    mixed_out = jnp.einsum("hqk,khd->qhd", rounded, values, preferred_element_type=jnp.float32)
    mixed_out = mixed_out / jnp.transpose(row_total, (1, 0, 2))
    return mixed_out.astype(jnp.bfloat16), query_seg


def sample_gates(cond, rows_weight):
    dp = ("dx", "dz")
    seg_count, model_width = cond.shape
    row_count = rows_weight.shape[0]
    nx = lax.axis_size("dx")
    nz = lax.axis_size("dz")
    col_block = model_width // nz
    feat_block = model_width // nx
    cond_act = jax.nn.silu(cond.astype(jnp.float32)).astype(jnp.bfloat16)
    w_cols = lax.all_to_all(
        rows_weight.reshape(row_count, nz, col_block), "dz", split_axis=1, concat_axis=0, tiled=True
    ).reshape(nz * row_count, col_block)
    sent = jnp.transpose(cond_act.reshape(seg_count, nx, feat_block), (1, 0, 2))
    sent = jnp.broadcast_to(sent[:, None], (nx, nz, seg_count, feat_block))
    feat = lax.all_to_all(
        sent.reshape(nx * nz, seg_count, feat_block), dp, split_axis=0, concat_axis=0, tiled=True
    ).reshape(nx * nz * seg_count, feat_block)
    partial = jnp.dot(feat, w_cols, preferred_element_type=jnp.float32)
    parts = lax.all_to_all(
        partial.reshape(nx * nz, seg_count, col_block), dp, split_axis=0, concat_axis=0, tiled=True
    )
    parts = parts.reshape(nx, nz, seg_count, col_block)
    summed = jnp.sum(parts, axis=0)
    return jnp.transpose(summed, (1, 0, 2)).reshape(seg_count, model_width)


def section_step(projected, seg_ids, condition, w_gate):
    tok_rows = projected.shape[2]
    head_count = projected.shape[4]
    head_size = projected.shape[5]
    model_width = head_count * head_size
    segment_row = seg_ids.reshape(-1)
    attended, local_segments = attend_chunk(projected[0, 0], segment_row, "sp")
    merged = attended.reshape(tok_rows, model_width)
    seg_line = jnp.zeros((1, model_width), jnp.bfloat16).at[0, :tok_rows].set(
        local_segments.astype(jnp.bfloat16)
    )
    packed = from_behind(jnp.concatenate([merged, seg_line], axis=0), "section", 1)
    merged = packed[:tok_rows]
    local_segments = packed[tok_rows, :tok_rows].astype(jnp.int32)
    seg_gate = from_behind(sample_gates(condition[0], w_gate[0]), "section", 1)
    seg_count = seg_gate.shape[0]
    one_hot = (local_segments[:, None] == jnp.arange(seg_count, dtype=jnp.int32)[None, :]).astype(
        jnp.float32
    )
    token_gate = jnp.dot(one_hot, seg_gate, precision=lax.Precision.HIGHEST)
    handed = (token_gate * merged.astype(jnp.float32)).astype(jnp.bfloat16)
    return handed.reshape(1, 1, tok_rows, model_width)


def solution(mesh):
    n_section, n_dp, n_sp = (mesh.shape[a] for a in ("section", "dp", "sp"))
    n_x = 4 if n_dp % 4 == 0 else 1
    split_mesh = Mesh(
        mesh.devices.reshape(n_section, n_x, n_dp // n_x, n_sp), ("section", "dx", "dz", "sp")
    )
    dp = ("dx", "dz")
    placed = (
        P("section", dp, "sp", None, None, None),
        P("section", dp, None),
        P("section", dp, None),
        P("section", dp, None),
    )
    return jax.shard_map(
        section_step,
        mesh=split_mesh,
        in_specs=placed,
        out_specs=P("section", dp, "sp", None),
        check_vma=False,
    )
```

```python
import math

import jax
import jax.numpy as jnp
from jax import lax
from jax.sharding import Mesh, PartitionSpec as P

masked_score = -1e30


def from_behind(block, axis, distance):
    devices = range(lax.axis_size(axis))
    route = [((i - distance) % len(devices), i) for i in devices]
    return lax.ppermute(block, axis, route)


def neighbour_keys(kv, axis):
    count = lax.axis_size(axis)
    from_left = lax.ppermute(kv, axis, [(i, i + 1) for i in range(count - 1)])
    from_right = lax.ppermute(kv, axis, [(i + 1, i) for i in range(count - 1)])
    return jnp.concatenate([from_left, kv, from_right], axis=0)


def attend_chunk(local, segment_row, axis):
    rows = local.shape[0]
    chunk = lax.axis_index(axis)
    total_rows = segment_row.shape[0]
    query_rows = local[:, 0]
    keys = neighbour_keys(local[:, 1:3], axis)
    key_rows = keys[:, 0]
    values = keys[:, 1]
    scale_factor = 1.0 / math.sqrt(query_rows.shape[2])
    query_seg = lax.dynamic_slice_in_dim(segment_row, chunk * rows, rows, 0)
    key_pos = (chunk - 1) * rows + jnp.arange(3 * rows, dtype=jnp.int32)
    key_valid = (key_pos >= 0) & (key_pos < total_rows)
    key_seg = jnp.take(segment_row, jnp.clip(key_pos, 0, total_rows - 1), axis=0)
    same_segment = (query_seg[:, None] == key_seg[None, :]) & key_valid[None, :]
    scores = (
        jnp.einsum("qhd,khd->hqk", query_rows, key_rows, preferred_element_type=jnp.float32)
        * scale_factor
    )
    scores = jnp.where(same_segment[None], scores, masked_score)
    row_max = jnp.max(scores, axis=2, keepdims=True)
    weights = jnp.exp(scores - row_max)
    row_total = jnp.sum(weights, axis=2, keepdims=True)
    rounded = weights.astype(jnp.bfloat16)
    mixed_out = jnp.einsum("hqk,khd->qhd", rounded, values, preferred_element_type=jnp.float32)
    mixed_out = mixed_out / jnp.transpose(row_total, (1, 0, 2))
    return mixed_out.astype(jnp.bfloat16), query_seg


def weight_columns(rows_weight):
    row_count, model_width = rows_weight.shape
    nz = lax.axis_size("dz")
    col_block = model_width // nz
    return lax.all_to_all(
        rows_weight.reshape(row_count, nz, col_block), "dz", split_axis=1, concat_axis=0, tiled=True
    ).reshape(nz * row_count, col_block)


def sample_gates(cond, w_cols):
    dp = ("dx", "dz")
    seg_count, model_width = cond.shape
    nx = lax.axis_size("dx")
    nz = lax.axis_size("dz")
    col_block = model_width // nz
    feat_block = model_width // nx
    cond_act = jax.nn.silu(cond.astype(jnp.float32)).astype(jnp.bfloat16)
    sent = jnp.transpose(cond_act.reshape(seg_count, nx, feat_block), (1, 0, 2))
    sent = jnp.broadcast_to(sent[:, None], (nx, nz, seg_count, feat_block))
    feat = lax.all_to_all(
        sent.reshape(nx * nz, seg_count, feat_block), dp, split_axis=0, concat_axis=0, tiled=True
    ).reshape(nx * nz * seg_count, feat_block)
    partial = jnp.dot(feat, w_cols, preferred_element_type=jnp.float32)
    parts = lax.all_to_all(
        partial.reshape(nx * nz, seg_count, col_block), dp, split_axis=0, concat_axis=0, tiled=True
    ).reshape(nx, nz, seg_count, col_block)
    summed = jnp.sum(parts, axis=0)
    return jnp.transpose(summed, (1, 0, 2)).reshape(seg_count, model_width)


def shards(projected, seg_ids, condition, w_gate):
    tok_rows = projected.shape[2]
    head_count = projected.shape[4]
    head_size = projected.shape[5]
    model_width = head_count * head_size
    segment_row = seg_ids.reshape(-1)
    attended, local_segments = attend_chunk(projected[0, 0], segment_row, "sp")
    merged = attended.reshape(tok_rows, model_width)
    seg_count = condition.shape[1]
    seg_line = jnp.zeros((1, model_width), jnp.bfloat16).at[0, :tok_rows].set(
        local_segments.astype(jnp.bfloat16)
    )
    packed = from_behind(jnp.concatenate([condition[0], seg_line], axis=0), "section", 1)
    local_segments = packed[seg_count, :tok_rows].astype(jnp.int32)
    w_cols = from_behind(weight_columns(w_gate[0]), "section", 1)
    seg_gate = sample_gates(packed[:seg_count], w_cols)
    merged = from_behind(merged, "section", 1)
    seg_count = seg_gate.shape[0]
    one_hot = (local_segments[:, None] == jnp.arange(seg_count, dtype=jnp.int32)[None, :]).astype(
        jnp.float32
    )
    token_gate = jnp.dot(one_hot, seg_gate, precision=lax.Precision.HIGHEST)
    handed = (token_gate * merged.astype(jnp.float32)).astype(jnp.bfloat16)
    return handed.reshape(1, 1, tok_rows, model_width)


def solution(mesh):
    n_section, n_dp, n_sp = (mesh.shape[a] for a in ("section", "dp", "sp"))
    n_x = 4 if n_dp % 4 == 0 else 1
    split_mesh = Mesh(
        mesh.devices.reshape(n_section, n_x, n_dp // n_x, n_sp), ("section", "dx", "dz", "sp")
    )
    dp = ("dx", "dz")
    placed = (
        P("section", dp, "sp", None, None, None),
        P("section", dp, None),
        P("section", dp, None),
        P("section", dp, None),
    )
    return jax.shard_map(
        shards,
        mesh=split_mesh,
        in_specs=placed,
        out_specs=P("section", dp, "sp", None),
        check_vma=False,
    )
```

```python
import math

import jax
import jax.numpy as jnp
from jax import lax
from jax.sharding import Mesh, PartitionSpec as P

masked_score = -1e30


def from_behind(block, axis, distance):
    devices = range(lax.axis_size(axis))
    route = [((i - distance) % len(devices), i) for i in devices]
    return lax.ppermute(block, axis, route)


def neighbour_keys(kv, axis):
    count = lax.axis_size(axis)
    from_left = lax.ppermute(kv, axis, [(i, i + 1) for i in range(count - 1)])
    from_right = lax.ppermute(kv, axis, [(i + 1, i) for i in range(count - 1)])
    return jnp.concatenate([from_left, kv, from_right], axis=0)


def attend_chunk(local, segment_row, axis):
    rows = local.shape[0]
    chunk = lax.axis_index(axis)
    total_rows = segment_row.shape[0]
    query_rows = local[:, 0]
    keys = neighbour_keys(local[:, 1:3], axis)
    key_rows = keys[:, 0]
    values = keys[:, 1]
    scale_factor = 1.0 / math.sqrt(query_rows.shape[2])
    query_seg = lax.dynamic_slice_in_dim(segment_row, chunk * rows, rows, 0)
    key_pos = (chunk - 1) * rows + jnp.arange(3 * rows, dtype=jnp.int32)
    key_valid = (key_pos >= 0) & (key_pos < total_rows)
    key_seg = jnp.take(segment_row, jnp.clip(key_pos, 0, total_rows - 1), axis=0)
    same_segment = (query_seg[:, None] == key_seg[None, :]) & key_valid[None, :]
    scores = (
        jnp.einsum("qhd,khd->hqk", query_rows, key_rows, preferred_element_type=jnp.float32)
        * scale_factor
    )
    scores = jnp.where(same_segment[None], scores, masked_score)
    row_max = jnp.max(scores, axis=2, keepdims=True)
    weights = jnp.exp(scores - row_max)
    row_total = jnp.sum(weights, axis=2, keepdims=True)
    rounded = weights.astype(jnp.bfloat16)
    mixed_out = jnp.einsum("hqk,khd->qhd", rounded, values, preferred_element_type=jnp.float32)
    mixed_out = mixed_out / jnp.transpose(row_total, (1, 0, 2))
    return mixed_out.astype(jnp.bfloat16), query_seg


def sample_gates(cond, rows_weight):
    dp = ("dx", "dz")
    seg_count, model_width = cond.shape
    row_count = rows_weight.shape[0]
    n_dp = model_width // row_count
    n_sp = lax.axis_size("sp")
    n_section = lax.axis_size("section")
    col_block = model_width // n_sp
    cond_act = jax.nn.silu(cond.astype(jnp.float32)).astype(jnp.bfloat16)
    feat = lax.all_to_all(
        cond_act.reshape(seg_count, n_dp, row_count), dp, split_axis=1, concat_axis=0, tiled=True
    ).reshape(n_dp * seg_count, row_count)
    cols = lax.dynamic_slice_in_dim(rows_weight, lax.axis_index("sp") * col_block, col_block, 1)
    partial = jnp.dot(feat, cols, preferred_element_type=jnp.float32).astype(jnp.bfloat16)
    parts = lax.all_to_all(
        partial.reshape(n_dp, seg_count, col_block), dp, split_axis=0, concat_axis=0, tiled=True
    )
    summed = jnp.sum(parts.astype(jnp.float32), axis=0)
    section = lax.axis_index("section")
    toward = (jnp.arange(n_section * n_sp, dtype=jnp.int32) // n_sp) == (section + 1) % n_section
    sent = jnp.where(toward[:, None, None], summed[None], 0.0)
    got = lax.all_to_all(sent, ("section", "sp"), split_axis=0, concat_axis=0, tiled=True)
    got = lax.dynamic_slice_in_dim(got, ((section + n_section - 1) % n_section) * n_sp, n_sp, 0)
    return jnp.transpose(got, (1, 0, 2)).reshape(seg_count, model_width)


def shards(projected, seg_ids, condition, w_gate):
    tok_rows = projected.shape[2]
    head_count = projected.shape[4]
    head_size = projected.shape[5]
    model_width = head_count * head_size
    segment_row = seg_ids.reshape(-1)
    attended, local_segments = attend_chunk(projected[0, 0], segment_row, "sp")
    merged = attended.reshape(tok_rows, model_width)
    seg_line = jnp.zeros((1, model_width), jnp.bfloat16).at[0, :tok_rows].set(
        local_segments.astype(jnp.bfloat16)
    )
    packed = from_behind(jnp.concatenate([merged, seg_line], axis=0), "section", 1)
    merged = packed[:tok_rows]
    local_segments = packed[tok_rows, :tok_rows].astype(jnp.int32)
    seg_gate = sample_gates(condition[0], w_gate[0])
    seg_count = seg_gate.shape[0]
    one_hot = (local_segments[:, None] == jnp.arange(seg_count, dtype=jnp.int32)[None, :]).astype(
        jnp.float32
    )
    token_gate = jnp.dot(one_hot, seg_gate, precision=lax.Precision.HIGHEST)
    handed = (token_gate * merged.astype(jnp.float32)).astype(jnp.bfloat16)
    return handed.reshape(1, 1, tok_rows, model_width)


def solution(mesh):
    n_section, n_dp, n_sp = (mesh.shape[a] for a in ("section", "dp", "sp"))
    n_x = 4 if n_dp % 4 == 0 else 1
    split_mesh = Mesh(
        mesh.devices.reshape(n_section, n_x, n_dp // n_x, n_sp), ("section", "dx", "dz", "sp")
    )
    dp = ("dx", "dz")
    placed = (
        P("section", dp, "sp", None, None, None),
        P("section", dp, None),
        P("section", dp, None),
        P("section", dp, None),
    )
    return jax.shard_map(
        shards,
        mesh=split_mesh,
        in_specs=placed,
        out_specs=P("section", dp, "sp", None),
        check_vma=False,
    )
```

```python
import math

import jax
import jax.numpy as jnp
from jax import lax
from jax.sharding import Mesh, PartitionSpec as P


masked_score = -1e30


def from_behind(block, axis, distance):
    devices = range(lax.axis_size(axis))
    route = [((i - distance) % len(devices), i) for i in devices]
    return lax.ppermute(block, axis, route)


def neighbour_keys(kv, axis):
    count = lax.axis_size(axis)
    from_left = lax.ppermute(kv, axis, [(i, i + 1) for i in range(count - 1)])
    from_right = lax.ppermute(kv, axis, [(i + 1, i) for i in range(count - 1)])
    return jnp.concatenate([from_left, kv, from_right], axis=0)


def attend_chunk(local, segment_row, axis):
    rows = local.shape[0]
    chunk = lax.axis_index(axis)
    total_rows = segment_row.shape[0]
    query_rows = local[:, 0]
    keys = neighbour_keys(local[:, 1:3], axis)
    key_rows = keys[:, 0]
    values = keys[:, 1]
    scale_factor = 1.0 / math.sqrt(query_rows.shape[2])
    query_seg = lax.dynamic_slice_in_dim(segment_row, chunk * rows, rows, 0)
    key_pos = (chunk - 1) * rows + jnp.arange(3 * rows, dtype=jnp.int32)
    key_valid = (key_pos >= 0) & (key_pos < total_rows)
    key_seg = jnp.take(segment_row, jnp.clip(key_pos, 0, total_rows - 1), axis=0)
    same_segment = (query_seg[:, None] == key_seg[None, :]) & key_valid[None, :]
    scores = (
        jnp.einsum("qhd,khd->hqk", query_rows, key_rows, preferred_element_type=jnp.float32)
        * scale_factor
    )
    scores = jnp.where(same_segment[None], scores, masked_score)
    row_max = jnp.max(scores, axis=2, keepdims=True)
    weights = jnp.exp(scores - row_max)
    row_total = jnp.sum(weights, axis=2, keepdims=True)
    rounded = weights.astype(jnp.bfloat16)
    mixed_out = jnp.einsum("hqk,khd->qhd", rounded, values, preferred_element_type=jnp.float32)
    mixed_out = mixed_out / jnp.transpose(row_total, (1, 0, 2))
    return mixed_out.astype(jnp.bfloat16), query_seg


def sample_gates(cond, rows_weight):
    dp = ("dx", "dz")
    seg_count, model_width = cond.shape
    row_count = rows_weight.shape[0]
    n_dp = model_width // row_count
    n_sp = lax.axis_size("sp")
    n_section = lax.axis_size("section")
    col_block = model_width // n_sp
    cond_act = jax.nn.silu(cond.astype(jnp.float32)).astype(jnp.bfloat16)
    feat = lax.all_to_all(
        cond_act.reshape(seg_count, n_dp, row_count), dp, split_axis=1, concat_axis=0, tiled=True
    )
    feat = feat.reshape(n_dp * seg_count, row_count)
    cols = lax.dynamic_slice_in_dim(rows_weight, lax.axis_index("sp") * col_block, col_block, 1)
    partial = jnp.dot(feat, cols, preferred_element_type=jnp.float32).astype(jnp.bfloat16)
    parts = lax.all_to_all(
        partial.reshape(n_dp, seg_count, col_block), dp, split_axis=0, concat_axis=0, tiled=True
    )
    summed = jnp.sum(parts.astype(jnp.float32), axis=0)
    section = lax.axis_index("section")
    toward = (jnp.arange(n_section * n_sp, dtype=jnp.int32) // n_sp) == (section + 1) % n_section
    sent = jnp.where(toward[:, None, None], summed[None], 0.0)
    got = lax.all_to_all(sent, ("section", "sp"), split_axis=0, concat_axis=0, tiled=True)
    got = lax.dynamic_slice_in_dim(got, ((section + n_section - 1) % n_section) * n_sp, n_sp, 0)
    return jnp.transpose(got, (1, 0, 2)).reshape(seg_count, model_width)


def section_step(projected, seg_ids, condition, w_gate):
    tok_rows = projected.shape[2]
    head_count = projected.shape[4]
    head_size = projected.shape[5]
    model_width = head_count * head_size
    segment_row = seg_ids.reshape(-1)
    attended, local_segments = attend_chunk(projected[0, 0], segment_row, "sp")
    merged = attended.reshape(tok_rows, model_width)
    seg_line = jnp.zeros((1, model_width), jnp.bfloat16).at[0, :tok_rows].set(
        local_segments.astype(jnp.bfloat16)
    )
    packed = from_behind(jnp.concatenate([merged, seg_line], axis=0), "section", 1)
    merged = packed[:tok_rows]
    local_segments = packed[tok_rows, :tok_rows].astype(jnp.int32)
    seg_gate = sample_gates(condition[0], w_gate[0])
    seg_count = seg_gate.shape[0]
    token_gate = jnp.broadcast_to(seg_gate[0][None, :], (tok_rows, model_width))
    for sample in range(1, seg_count):
        token_gate = jnp.where(
            (local_segments == sample)[:, None], seg_gate[sample][None, :], token_gate
        )
    handed = (token_gate * merged.astype(jnp.float32)).astype(jnp.bfloat16)
    return handed.reshape(1, 1, tok_rows, model_width)


def solution(mesh):
    n_section, n_dp, n_sp = (mesh.shape[a] for a in ("section", "dp", "sp"))
    n_x = 4 if n_dp % 4 == 0 else 1
    split_mesh = Mesh(
        mesh.devices.reshape(n_section, n_x, n_dp // n_x, n_sp), ("section", "dx", "dz", "sp")
    )
    dp = ("dx", "dz")
    placed = (
        P("section", dp, "sp", None, None, None),
        P("section", dp, None),
        P("section", dp, None),
        P("section", dp, None),
    )
    return jax.shard_map(
        section_step,
        mesh=split_mesh,
        in_specs=placed,
        out_specs=P("section", dp, "sp", None),
        check_vma=False,
    )
```

```python
import math

import jax
import jax.numpy as jnp
from jax import lax
from jax.sharding import Mesh, PartitionSpec as P

masked_score = -1e30


def from_behind(block, axis, distance):
    devices = range(lax.axis_size(axis))
    route = [((i - distance) % len(devices), i) for i in devices]
    return lax.ppermute(block, axis, route)


def neighbour_keys(kv, axis):
    count = lax.axis_size(axis)
    from_left = lax.ppermute(kv, axis, [(i, i + 1) for i in range(count - 1)])
    from_right = lax.ppermute(kv, axis, [(i + 1, i) for i in range(count - 1)])
    return jnp.concatenate([from_left, kv, from_right], axis=0)


def attend_chunk(local, segment_row, axis):
    rows = local.shape[0]
    chunk = lax.axis_index(axis)
    total_rows = segment_row.shape[0]
    query_rows = local[:, 0]
    keys = neighbour_keys(local[:, 1:3], axis)
    key_rows = keys[:, 0]
    values = keys[:, 1]
    scale_factor = 1.0 / math.sqrt(query_rows.shape[2])
    query_seg = lax.dynamic_slice_in_dim(segment_row, chunk * rows, rows, 0)
    key_pos = (chunk - 1) * rows + jnp.arange(3 * rows, dtype=jnp.int32)
    key_valid = (key_pos >= 0) & (key_pos < total_rows)
    key_seg = jnp.take(segment_row, jnp.clip(key_pos, 0, total_rows - 1), axis=0)
    same_segment = (query_seg[:, None] == key_seg[None, :]) & key_valid[None, :]
    scores = (
        jnp.einsum("qhd,khd->hqk", query_rows, key_rows, preferred_element_type=jnp.float32)
        * scale_factor
    )
    scores = jnp.where(same_segment[None], scores, masked_score)
    row_max = jnp.max(scores, axis=2, keepdims=True)
    weights = jnp.exp(scores - row_max)
    row_total = jnp.sum(weights, axis=2, keepdims=True)
    rounded = weights.astype(jnp.bfloat16)
    mixed_out = jnp.einsum("hqk,khd->qhd", rounded, values, preferred_element_type=jnp.float32)
    mixed_out = mixed_out / jnp.transpose(row_total, (1, 0, 2))
    return mixed_out.astype(jnp.bfloat16), query_seg


def sample_gates(cond, rows_weight):
    dp = ("dx", "dz")
    seg_count, model_width = cond.shape
    row_count = rows_weight.shape[0]
    n_dp = model_width // row_count
    n_sp = lax.axis_size("sp")
    n_section = lax.axis_size("section")
    col_block = model_width // n_sp
    cond_act = jax.nn.silu(cond.astype(jnp.float32)).astype(jnp.bfloat16)
    feat = lax.all_to_all(
        cond_act.reshape(seg_count, n_dp, row_count), dp, split_axis=1, concat_axis=0, tiled=True
    ).reshape(n_dp * seg_count, row_count)
    cols = lax.dynamic_slice_in_dim(rows_weight, lax.axis_index("sp") * col_block, col_block, 1)
    partial = jnp.dot(feat, cols, preferred_element_type=jnp.float32)
    parts = lax.all_to_all(
        partial.reshape(n_dp, seg_count, col_block), dp, split_axis=0, concat_axis=0, tiled=True
    )
    summed = jnp.sum(parts, axis=0)
    section = lax.axis_index("section")
    toward = (jnp.arange(n_section * n_sp, dtype=jnp.int32) // n_sp) == (section + 1) % n_section
    sent = jnp.where(toward[:, None, None], summed[None], 0.0)
    got = lax.all_to_all(sent, ("section", "sp"), split_axis=0, concat_axis=0, tiled=True)
    got = lax.dynamic_slice_in_dim(got, ((section + n_section - 1) % n_section) * n_sp, n_sp, 0)
    return jnp.transpose(got, (1, 0, 2)).reshape(seg_count, model_width)


def shards(projected, seg_ids, condition, w_gate):
    tok_rows = projected.shape[2]
    head_count = projected.shape[4]
    head_size = projected.shape[5]
    model_width = head_count * head_size
    segment_row = seg_ids.reshape(-1)
    attended, local_segments = attend_chunk(projected[0, 0], segment_row, "sp")
    merged = attended.reshape(tok_rows, model_width)
    seg_line = jnp.zeros((1, model_width), jnp.bfloat16).at[0, :tok_rows].set(
        local_segments.astype(jnp.bfloat16)
    )
    packed = from_behind(jnp.concatenate([merged, seg_line], axis=0), "section", 1)
    merged = packed[:tok_rows]
    local_segments = packed[tok_rows, :tok_rows].astype(jnp.int32)
    seg_gate = sample_gates(condition[0], w_gate[0])
    seg_count = seg_gate.shape[0]
    one_hot = (local_segments[:, None] == jnp.arange(seg_count, dtype=jnp.int32)[None, :]).astype(
        jnp.float32
    )
    token_gate = jnp.dot(one_hot, seg_gate, precision=lax.Precision.HIGHEST)
    handed = (token_gate * merged.astype(jnp.float32)).astype(jnp.bfloat16)
    return handed.reshape(1, 1, tok_rows, model_width)


def solution(mesh):
    n_section, n_dp, n_sp = (mesh.shape[a] for a in ("section", "dp", "sp"))
    n_x = 4 if n_dp % 4 == 0 else 1
    split_mesh = Mesh(
        mesh.devices.reshape(n_section, n_x, n_dp // n_x, n_sp), ("section", "dx", "dz", "sp")
    )
    dp = ("dx", "dz")
    placed = (
        P("section", dp, "sp", None, None, None),
        P("section", dp, None),
        P("section", dp, None),
        P("section", dp, None),
    )
    return jax.shard_map(
        shards,
        mesh=split_mesh,
        in_specs=placed,
        out_specs=P("section", dp, "sp", None),
        check_vma=False,
    )
```

```python
import math

import jax
import jax.numpy as jnp
from jax import lax
from jax.sharding import Mesh, PartitionSpec as P

masked_score = -1e30


def from_behind(block, axis, distance):
    devices = range(lax.axis_size(axis))
    route = [((i - distance) % len(devices), i) for i in devices]
    return lax.ppermute(block, axis, route)


def neighbour_keys(kv, axis):
    count = lax.axis_size(axis)
    from_left = lax.ppermute(kv, axis, [(i, i + 1) for i in range(count - 1)])
    from_right = lax.ppermute(kv, axis, [(i + 1, i) for i in range(count - 1)])
    return jnp.concatenate([from_left, kv, from_right], axis=0)


def attend_chunk(local, segment_row, axis):
    rows = local.shape[0]
    chunk = lax.axis_index(axis)
    total_rows = segment_row.shape[0]
    query_rows = local[:, 0]
    keys = neighbour_keys(local[:, 1:3], axis)
    key_rows = keys[:, 0]
    values = keys[:, 1]
    scale_factor = 1.0 / math.sqrt(query_rows.shape[2])
    query_seg = lax.dynamic_slice_in_dim(segment_row, chunk * rows, rows, 0)
    key_pos = (chunk - 1) * rows + jnp.arange(3 * rows, dtype=jnp.int32)
    key_valid = (key_pos >= 0) & (key_pos < total_rows)
    key_seg = jnp.take(segment_row, jnp.clip(key_pos, 0, total_rows - 1), axis=0)
    same_segment = (query_seg[:, None] == key_seg[None, :]) & key_valid[None, :]
    scores = (
        jnp.einsum("qhd,khd->hqk", query_rows, key_rows, preferred_element_type=jnp.float32)
        * scale_factor
    )
    scores = jnp.where(same_segment[None], scores, masked_score)
    row_max = jnp.max(scores, axis=2, keepdims=True)
    weights = jnp.exp(scores - row_max)
    row_total = jnp.sum(weights, axis=2, keepdims=True)
    rounded = weights.astype(jnp.bfloat16)
    mixed_out = jnp.einsum("hqk,khd->qhd", rounded, values, preferred_element_type=jnp.float32)
    mixed_out = mixed_out / jnp.transpose(row_total, (1, 0, 2))
    return mixed_out.astype(jnp.bfloat16), query_seg


def sample_gates(cond, rows_weight):
    dp = ("dx", "dz")
    seg_count, model_width = cond.shape
    row_count = rows_weight.shape[0]
    nx = lax.axis_size("dx")
    nz = lax.axis_size("dz")
    n_sp = lax.axis_size("sp")
    n_section = lax.axis_size("section")
    col_block = model_width // (nz * n_sp)
    feat_block = model_width // nx
    cond_act = jax.nn.silu(cond.astype(jnp.float32)).astype(jnp.bfloat16)
    mine = lax.dynamic_index_in_dim(
        rows_weight.reshape(row_count, nz, n_sp, col_block), lax.axis_index("sp"), axis=2,
        keepdims=False,
    )
    w_cols = lax.all_to_all(mine, "dz", split_axis=1, concat_axis=0, tiled=True).reshape(
        nz * row_count, col_block
    )
    sent = jnp.transpose(cond_act.reshape(seg_count, nx, feat_block), (1, 0, 2))
    sent = jnp.broadcast_to(sent[:, None], (nx, nz, seg_count, feat_block))
    feat = lax.all_to_all(
        sent.reshape(nx * nz, seg_count, feat_block), dp, split_axis=0, concat_axis=0, tiled=True
    ).reshape(nx * nz * seg_count, feat_block)
    partial = jnp.dot(feat, w_cols, preferred_element_type=jnp.float32)
    parts = lax.all_to_all(
        partial.reshape(nx * nz, seg_count, col_block), dp, split_axis=0, concat_axis=0, tiled=True
    ).reshape(nx, nz, seg_count, col_block)
    summed = jnp.sum(parts, axis=0)
    section = lax.axis_index("section")
    toward = (jnp.arange(n_section * n_sp, dtype=jnp.int32) // n_sp) == (section + 1) % n_section
    sent = jnp.where(toward[:, None, None, None], summed[None], 0.0)
    got = lax.all_to_all(sent, ("section", "sp"), split_axis=0, concat_axis=0, tiled=True)
    got = lax.dynamic_slice_in_dim(got, ((section + n_section - 1) % n_section) * n_sp, n_sp, 0)
    return jnp.transpose(got, (2, 1, 0, 3)).reshape(seg_count, model_width)


def shards(projected, seg_ids, condition, w_gate):
    tok_rows = projected.shape[2]
    head_count = projected.shape[4]
    head_size = projected.shape[5]
    model_width = head_count * head_size
    segment_row = seg_ids.reshape(-1)
    attended, local_segments = attend_chunk(projected[0, 0], segment_row, "sp")
    merged = attended.reshape(tok_rows, model_width)
    seg_line = jnp.zeros((1, model_width), jnp.bfloat16).at[0, :tok_rows].set(
        local_segments.astype(jnp.bfloat16)
    )
    packed = from_behind(jnp.concatenate([merged, seg_line], axis=0), "section", 1)
    merged = packed[:tok_rows]
    local_segments = packed[tok_rows, :tok_rows].astype(jnp.int32)
    seg_gate = sample_gates(condition[0], w_gate[0])
    seg_count = seg_gate.shape[0]
    one_hot = (local_segments[:, None] == jnp.arange(seg_count, dtype=jnp.int32)[None, :]).astype(
        jnp.float32
    )
    token_gate = jnp.dot(one_hot, seg_gate, precision=lax.Precision.HIGHEST)
    handed = (token_gate * merged.astype(jnp.float32)).astype(jnp.bfloat16)
    return handed.reshape(1, 1, tok_rows, model_width)


def solution(mesh):
    n_section, n_dp, n_sp = (mesh.shape[a] for a in ("section", "dp", "sp"))
    n_x = 4 if n_dp % 4 == 0 else 1
    split_mesh = Mesh(
        mesh.devices.reshape(n_section, n_x, n_dp // n_x, n_sp), ("section", "dx", "dz", "sp")
    )
    dp = ("dx", "dz")
    placed = (
        P("section", dp, "sp", None, None, None),
        P("section", dp, None),
        P("section", dp, None),
        P("section", dp, None),
    )
    return jax.shard_map(
        shards,
        mesh=split_mesh,
        in_specs=placed,
        out_specs=P("section", dp, "sp", None),
        check_vma=False,
    )
```

```python
import math

import jax
import jax.numpy as jnp
from jax import lax
from jax.sharding import Mesh, PartitionSpec as P

masked_score = -1e30


def from_behind(block, axis, distance):
    devices = range(lax.axis_size(axis))
    route = [((i - distance) % len(devices), i) for i in devices]
    return lax.ppermute(block, axis, route)


def neighbour_keys(kv, axis):
    count = lax.axis_size(axis)
    from_left = lax.ppermute(kv, axis, [(i, i + 1) for i in range(count - 1)])
    from_right = lax.ppermute(kv, axis, [(i + 1, i) for i in range(count - 1)])
    return jnp.concatenate([from_left, kv, from_right], axis=0)


def attend_chunk(local, segment_row, axis):
    rows = local.shape[0]
    chunk = lax.axis_index(axis)
    total_rows = segment_row.shape[0]
    query_rows = local[:, 0]
    keys = neighbour_keys(local[:, 1:3], axis)
    key_rows = keys[:, 0]
    values = keys[:, 1]
    scale_factor = 1.0 / math.sqrt(query_rows.shape[2])
    query_seg = lax.dynamic_slice_in_dim(segment_row, chunk * rows, rows, 0)
    key_pos = (chunk - 1) * rows + jnp.arange(3 * rows, dtype=jnp.int32)
    key_valid = (key_pos >= 0) & (key_pos < total_rows)
    key_seg = jnp.take(segment_row, jnp.clip(key_pos, 0, total_rows - 1), axis=0)
    same_segment = (query_seg[:, None] == key_seg[None, :]) & key_valid[None, :]
    scores = (
        jnp.einsum("qhd,khd->hqk", query_rows, key_rows, preferred_element_type=jnp.float32)
        * scale_factor
    )
    scores = jnp.where(same_segment[None], scores, masked_score)
    row_max = jnp.max(scores, axis=2, keepdims=True)
    weights = jnp.exp(scores - row_max)
    row_total = jnp.sum(weights, axis=2, keepdims=True)
    rounded = weights.astype(jnp.bfloat16)
    mixed_out = jnp.einsum("hqk,khd->qhd", rounded, values, preferred_element_type=jnp.float32)
    mixed_out = mixed_out / jnp.transpose(row_total, (1, 0, 2))
    return mixed_out.astype(jnp.bfloat16), query_seg


def sample_gates(cond, rows_weight):
    dp = ("dx", "dz")
    seg_count, model_width = cond.shape
    row_count = rows_weight.shape[0]
    nx = lax.axis_size("dx")
    nz = lax.axis_size("dz")
    n_sp = lax.axis_size("sp")
    n_section = lax.axis_size("section")
    col_block = model_width // (nz * n_sp)
    feat_block = model_width // nx
    cond_act = jax.nn.silu(cond.astype(jnp.float32)).astype(jnp.bfloat16)
    mine = lax.dynamic_index_in_dim(
        rows_weight.reshape(row_count, nz, n_sp, col_block), lax.axis_index("sp"), axis=2,
        keepdims=False,
    )
    act_part = jnp.transpose(cond_act.reshape(seg_count, nx, feat_block), (1, 0, 2))
    act_part = jnp.broadcast_to(
        act_part.reshape(nx, 1, seg_count * feat_block), (nx, nz, seg_count * feat_block)
    )
    w_part = jnp.transpose(mine, (1, 0, 2)).reshape(1, nz, row_count * col_block)
    my_x = lax.axis_index("dx")
    same_x = (jnp.arange(nx, dtype=jnp.int32) == my_x)[:, None, None]
    w_part = jnp.where(same_x, w_part, jnp.zeros_like(w_part))
    sent = jnp.concatenate([act_part, w_part], axis=2).reshape(nx * nz, -1)
    got = lax.all_to_all(sent, dp, split_axis=0, concat_axis=0, tiled=True)
    act_size = seg_count * feat_block
    feat = got[:, :act_size].reshape(nx * nz * seg_count, feat_block)
    w_cols = lax.dynamic_index_in_dim(
        got[:, act_size:].reshape(nx, nz, row_count * col_block), my_x, axis=0, keepdims=False
    ).reshape(nz * row_count, col_block)
    partial = jnp.dot(feat, w_cols, preferred_element_type=jnp.float32)
    parts = lax.all_to_all(
        partial.reshape(nx * nz, seg_count, col_block), dp, split_axis=0, concat_axis=0, tiled=True
    ).reshape(nx, nz, seg_count, col_block)
    summed = jnp.sum(parts, axis=0)
    section = lax.axis_index("section")
    toward = (jnp.arange(n_section * n_sp, dtype=jnp.int32) // n_sp) == (section + 1) % n_section
    sent = jnp.where(toward[:, None, None, None], summed[None], 0.0)
    got = lax.all_to_all(sent, ("section", "sp"), split_axis=0, concat_axis=0, tiled=True)
    got = lax.dynamic_slice_in_dim(got, ((section + n_section - 1) % n_section) * n_sp, n_sp, 0)
    return jnp.transpose(got, (2, 1, 0, 3)).reshape(seg_count, model_width)


def shards(projected, seg_ids, condition, w_gate):
    tok_rows = projected.shape[2]
    head_count = projected.shape[4]
    head_size = projected.shape[5]
    model_width = head_count * head_size
    segment_row = seg_ids.reshape(-1)
    attended, local_segments = attend_chunk(projected[0, 0], segment_row, "sp")
    merged = attended.reshape(tok_rows, model_width)
    seg_line = jnp.zeros((1, model_width), jnp.bfloat16).at[0, :tok_rows].set(
        local_segments.astype(jnp.bfloat16)
    )
    packed = from_behind(jnp.concatenate([merged, seg_line], axis=0), "section", 1)
    merged = packed[:tok_rows]
    local_segments = packed[tok_rows, :tok_rows].astype(jnp.int32)
    seg_gate = sample_gates(condition[0], w_gate[0])
    seg_count = seg_gate.shape[0]
    one_hot = (local_segments[:, None] == jnp.arange(seg_count, dtype=jnp.int32)[None, :]).astype(
        jnp.float32
    )
    token_gate = jnp.dot(one_hot, seg_gate, precision=lax.Precision.HIGHEST)
    handed = (token_gate * merged.astype(jnp.float32)).astype(jnp.bfloat16)
    return handed.reshape(1, 1, tok_rows, model_width)


def solution(mesh):
    n_section, n_dp, n_sp = (mesh.shape[a] for a in ("section", "dp", "sp"))
    n_x = 4 if n_dp % 4 == 0 else 1
    split_mesh = Mesh(
        mesh.devices.reshape(n_section, n_x, n_dp // n_x, n_sp), ("section", "dx", "dz", "sp")
    )
    dp = ("dx", "dz")
    placed = (
        P("section", dp, "sp", None, None, None),
        P("section", dp, None),
        P("section", dp, None),
        P("section", dp, None),
    )
    return jax.shard_map(
        shards,
        mesh=split_mesh,
        in_specs=placed,
        out_specs=P("section", dp, "sp", None),
        check_vma=False,
    )
```
